512 devices in a mesh: table: 64 (over z, x, core), dp: 8 (over y).
Axes of the slice: x: 4, y: 8, z: 8, core: 2. Of those that a mesh axis runs over, the one named last changes fastest.
Arguments:
- user_table: bfloat16 [32768, 128], P('table'), may hold values from -6 to 6
- item_table: bfloat16 [32768, 128], P('table'), may hold values from -6 to 6
- user_pick: int32 [64, 8, 64, 16], P('table', 'dp'), may hold values from 0 to 511
- item_pick: int32 [64, 8, 64, 20], P('table', 'dp'), may hold values from 0 to 511
- user_slot: int32 [64, 8, 64, 16], P('table', 'dp'), may hold values from -1 to 255, as said below
- item_slot: int32 [64, 8, 64, 20], P('table', 'dp'), may hold values from -1 to 319, as said below
- user_w1: bfloat16 [256, 1024], replicated, may hold values from -0.375 to 0.375
- user_w2: bfloat16 [1024, 128], replicated, may hold values from -0.1875 to 0.1875
- item_w1: bfloat16 [256, 1024], replicated, may hold values from -0.375 to 0.375
- item_w2: bfloat16 [1024, 128], replicated, may hold values from -0.1875 to 0.1875
Outputs:
- user_table_grad: float32 [32768, 128], P(('table', 'dp'))
- item_table_grad: float32 [32768, 128], P(('table', 'dp'))
- user_w1_grad: bfloat16 [256, 1024], replicated
- user_w2_grad: bfloat16 [1024, 128], replicated
- item_w1_grad: bfloat16 [256, 1024], replicated
- item_w2_grad: bfloat16 [1024, 128], replicated
The draws below stay inside these ranges and needn't reach their ends.
Inputs may be any that keep to these rules, and one draw needn't show every extreme that they name: `user_slot`: in each bucket of 16 slots from one device to one shard the occupied slots come first and the others hold -1; for every index along dp some shard receives full buckets from every device of that index. `item_slot`: in each bucket of 20 slots from one device to one shard the occupied slots come first and the others hold -1; for every index along dp some shard receives full buckets from every device of that index.
All inputs are finite; a program needn't handle non-finite values.
Results may differ from the reference program's by a relative error of at most 0.012.
The reference program's roundings to bfloat16 on the way count: a program that leaves them out, or rounds other values in their place, can miss the bound.
Values may be sent and summed in bfloat16 or wider, within the bound.
No kernel may reach another device: no remote copies, remote signals or barrier semaphores. Data moves between devices by JAX's collectives and lax.ppermute only.
A program may use at most 64 MiB of HBM per device.

```python
import math
import jax
import jax.numpy as jnp
import numpy as np
from jax import lax

E = 128
FEATS = 2
HID = 1024
OUT = 128
B_DEV = 128
NEG_DEV = 32
ROWS_DEV = 512
SHARDS = 64
REPLICAS = 8
CAP_U = 16
CAP_I = 20
ROWS = 32768


def bucket_segments(key, capacity, segment_count):
    key_hot, key_count, key_segment = jax.random.split(key, 3)
    hot_owner = jax.random.randint(key_hot, (REPLICAS,), 0, SHARDS)
    counts = jax.random.randint(key_count, (SHARDS, REPLICAS, SHARDS), capacity // 4, 5 * capacity // 8 + 1)
    owners = jnp.arange(SHARDS)
    full_bucket = owners[None, None, :] == hot_owner[None, :, None]
    counts = jnp.where(full_bucket, capacity, counts)
    segment = jax.random.randint(key_segment, (SHARDS, REPLICAS, SHARDS, capacity), 0, segment_count)
    occupied = jnp.arange(capacity)[None, None, None, :] < counts[..., None]
    return jnp.where(occupied, segment, -1).astype(jnp.int32)


def draw_user_slot(key, part):
    return bucket_segments(jax.random.fold_in(key, 11), CAP_U, B_DEV * FEATS)


def draw_item_slot(key, part):
    return bucket_segments(jax.random.fold_in(key, 23), CAP_I, (B_DEV + NEG_DEV) * FEATS)


def place_ends(values, rng, least, largest):
    spot = [jax.random.randint(jax.random.fold_in(rng, axis), (), 0, length) for axis, length in enumerate(values.shape)]
    longest = values.shape.index(max(values.shape))
    beside = spot[:longest] + [(spot[longest] + 1) % values.shape[longest]] + spot[longest + 1:]
    return values.at[tuple(spot)].set(least).at[tuple(beside)].set(largest)


def level_of(key, shape, pieces, low, high):
    def one(position, shards_of):
        draws = jax.random.uniform(jax.random.fold_in(jax.random.fold_in(key, 6), position), (shards_of,), jnp.float32, low / len(pieces), high / len(pieces))
        return jnp.repeat(jnp.exp(draws), shape[position] // shards_of).reshape((-1,) + (1,) * (len(shape) - position - 1))

    factor_of = one(*pieces[0])
    for cut in pieces[1:]:
        factor_of = factor_of * one(*cut)
    return factor_of


def rank_table(number_of, slope):
    loads = [(1 << 20) // math.isqrt(grade ** slope) + 1 for grade in range(1, number_of + 1)]
    deviation = 1 + sum(loads) // (1 << 30)
    return np.cumsum(np.array([max(1, weight // deviation) for weight in loads]))


def ranked(stream_key, dims, number_of, slope):
    listing = rank_table(number_of, slope)
    ticket = jax.random.randint(jax.random.fold_in(stream_key, 1), dims, 0, int(listing[number_of - 1]))
    rank = jnp.searchsorted(jnp.asarray(listing, jnp.int32), ticket, side="right")
    return jax.random.permutation(jax.random.fold_in(stream_key, 2), number_of)[rank].astype(jnp.int32)


def normal_values(key, extent, width, limit, cuts=(), kind=jnp.bfloat16):
    loudness = level_of(key, extent, cuts, -0.22, 0.18) if cuts else 1.0
    array = jax.random.normal(key, extent, jnp.float32) * width * loudness
    return jnp.minimum(jnp.maximum(array, -limit), limit).astype(kind)


def setup_inputs(seed: int = 0) -> dict:
    key_of = jax.random.split(jax.random.key(seed), 11)
    user_table = normal_values(key_of[0], (ROWS, E), 1.0, 6.0, ((0, 64),))
    item_table = normal_values(key_of[1], (ROWS, E), 1.0, 6.0, ((0, 64),))
    user_pick = place_ends(ranked(key_of[2], (SHARDS, REPLICAS, SHARDS, CAP_U), ROWS_DEV, 2), jax.random.fold_in(key_of[2], 3), 0, ROWS_DEV - 1).astype(jnp.int32)
    item_pick = place_ends(ranked(key_of[3], (SHARDS, REPLICAS, SHARDS, CAP_I), ROWS_DEV, 2), jax.random.fold_in(key_of[3], 3), 0, ROWS_DEV - 1).astype(jnp.int32)
    user_slot = draw_user_slot(jax.random.fold_in(key_of[10], 71), 0)
    item_slot = draw_item_slot(jax.random.fold_in(key_of[10], 71), 0)
    user_w1 = normal_values(key_of[6], (FEATS * E, HID), (FEATS * E) ** -0.5, 0.375)
    user_w2 = normal_values(key_of[7], (HID, OUT), HID ** -0.5, 0.1875)
    item_w1 = normal_values(key_of[8], (FEATS * E, HID), (FEATS * E) ** -0.5, 0.375)
    item_w2 = normal_values(key_of[9], (HID, OUT), HID ** -0.5, 0.1875)
    return dict(user_table=user_table, item_table=item_table, user_pick=user_pick, item_pick=item_pick, user_slot=user_slot, item_slot=item_slot, user_w1=user_w1, user_w2=user_w2, item_w1=item_w1, item_w2=item_w2)


score_divisor_scale = 0.05
epsilon = 1e-06

def pool_rows(table, pick, slot, seg_total):
    shard_base = (jnp.arange(SHARDS, dtype=jnp.int32) * ROWS_DEV)[:, None, None, None]
    global_rows = jnp.transpose(pick + shard_base, (2, 1, 0, 3)).reshape(SHARDS * REPLICAS, -1)
    slot_flat = slot.reshape(SHARDS * REPLICAS, -1)

    def one_device(inputs_pair):
        row_ids, seg_ids = inputs_pair
        values = table[row_ids].astype(jnp.float32)
        labels = jnp.where(seg_ids < 0, seg_total, seg_ids)
        summed = jax.ops.segment_sum(values, labels, num_segments=seg_total + 1)
        return summed[:seg_total].astype(jnp.bfloat16)
    return (lax.map(one_device, (global_rows, slot_flat)), global_rows, slot_flat)

def tower_forward(inputs, first_weight, second_weight):
    preact = jnp.dot(inputs, first_weight, preferred_element_type=jnp.float32)
    hidden = jnp.maximum(preact, 0.0).astype(jnp.bfloat16)
    output = jnp.dot(hidden, second_weight, preferred_element_type=jnp.float32)
    magnitude = jnp.sqrt(lax.optimization_barrier(jnp.sum(output * output, axis=-1, keepdims=True)) + epsilon)
    unit_vec = output / magnitude
    return (preact, hidden, magnitude, unit_vec, unit_vec.astype(jnp.bfloat16))

def tower_backward(inputs, first_weight, second_weight, preact, hidden, magnitude, unit_vec, emb_gradient):
    along = lax.optimization_barrier(jnp.sum(unit_vec * emb_gradient, axis=-1, keepdims=True))
    out_gradient = ((emb_gradient - unit_vec * along) / magnitude).astype(jnp.bfloat16)
    second_grad = jnp.dot(hidden.T, out_gradient, preferred_element_type=jnp.float32)
    back_hidden = jnp.dot(out_gradient, second_weight.T, preferred_element_type=jnp.float32)
    hidden_grad = jnp.where(preact > 0, back_hidden, 0.0).astype(jnp.bfloat16)
    first_grad = jnp.dot(inputs.T, hidden_grad, preferred_element_type=jnp.float32)
    input_grad = jnp.dot(hidden_grad, first_weight.T, preferred_element_type=jnp.float32).astype(jnp.bfloat16)
    return (first_grad, second_grad, input_grad)

def table_gradient(global_rows, slot_flat, input_grads):

    def add_device(running, triple):
        row_ids, seg_ids, gradient = triple
        clamped = jnp.maximum(seg_ids, 0)
        values = jnp.where((seg_ids >= 0)[:, None], gradient[clamped].astype(jnp.float32), 0.0)
        return (running.at[row_ids].add(values), None)
    start_total = jnp.zeros((ROWS, E), jnp.float32)
    result, _ = lax.scan(add_device, start_total, (global_rows, slot_flat, input_grads))
    return result

def reference(user_table, item_table, user_pick, item_pick, user_slot, item_slot, user_w1, user_w2, item_w1, item_w2):
    item_rows = B_DEV + NEG_DEV
    user_pooled, user_global, user_flat = pool_rows(user_table, user_pick, user_slot, B_DEV * FEATS)
    item_pooled, item_global, item_flat = pool_rows(item_table, item_pick, item_slot, item_rows * FEATS)
    user_groups = user_pooled.reshape(SHARDS, REPLICAS * B_DEV, FEATS * E)
    item_groups = item_pooled.reshape(SHARDS, REPLICAS * item_rows, FEATS * E)
    columns = jnp.arange(REPLICAS * item_rows, dtype=jnp.int32)
    user_index = jnp.arange(REPLICAS * B_DEV, dtype=jnp.int32)
    positive = user_index // B_DEV * item_rows + user_index % B_DEV
    correct_class_indices = (columns[None, :] == positive[:, None]).astype(jnp.float32)

    def group_step(running, inputs_pair):
        user_input, item_input = inputs_pair
        user_state = tower_forward(user_input, user_w1, user_w2)
        item_state = tower_forward(item_input, item_w1, item_w2)
        query_embedding_matrix = user_state[4]
        candidate_embedding_matrix = item_state[4]
        pairwise_match_scores = jnp.dot(query_embedding_matrix, candidate_embedding_matrix.T, preferred_element_type=jnp.float32) / score_divisor_scale
        exponent = jnp.exp(pairwise_match_scores)
        learnable_model_state = exponent / lax.optimization_barrier(jnp.sum(exponent, axis=1, keepdims=True))
        score_derivative_matrix = ((learnable_model_state - correct_class_indices) / score_divisor_scale).astype(jnp.bfloat16)
        user_emb_grad = jnp.dot(score_derivative_matrix, candidate_embedding_matrix, preferred_element_type=jnp.float32)
        item_emb_grad = jnp.dot(score_derivative_matrix.T, query_embedding_matrix, preferred_element_type=jnp.float32)
        user_back = tower_backward(user_input, user_w1, user_w2, user_state[0], user_state[1], user_state[2], user_state[3], user_emb_grad)
        item_back = tower_backward(item_input, item_w1, item_w2, item_state[0], item_state[1], item_state[2], item_state[3], item_emb_grad)
        updated = (running[0] + user_back[0], running[1] + user_back[1], running[2] + item_back[0], running[3] + item_back[1])
        return (updated, (user_back[2], item_back[2]))
    start_sums = (jnp.zeros((FEATS * E, HID), jnp.float32), jnp.zeros((HID, OUT), jnp.float32), jnp.zeros((FEATS * E, HID), jnp.float32), jnp.zeros((HID, OUT), jnp.float32))
    weight_sums, input_grads = lax.scan(group_step, start_sums, (user_groups, item_groups))
    user_in_grad = input_grads[0].reshape(SHARDS * REPLICAS, B_DEV * FEATS, E)
    item_in_grad = input_grads[1].reshape(SHARDS * REPLICAS, item_rows * FEATS, E)
    user_table_grad = table_gradient(user_global, user_flat, user_in_grad)
    item_table_grad = table_gradient(item_global, item_flat, item_in_grad)
    return (user_table_grad, item_table_grad, weight_sums[0].astype(jnp.bfloat16), weight_sums[1].astype(jnp.bfloat16), weight_sums[2].astype(jnp.bfloat16), weight_sums[3].astype(jnp.bfloat16))
```

```python
import jax
import jax.numpy as jnp
from jax import lax
from jax.sharding import PartitionSpec as P

FEATS = 2
B_DEV = 128
NEG_DEV = 32


score_divisor_scale = 0.05
epsilon = 1e-06


def tower_forward(inputs, first_weight, second_weight):
    preact = jnp.dot(inputs, first_weight, preferred_element_type=jnp.float32)
    hidden = jnp.maximum(preact, 0.0).astype(jnp.bfloat16)
    output = jnp.dot(hidden, second_weight, preferred_element_type=jnp.float32)
    magnitude = jnp.sqrt(jnp.sum(output * output, axis=-1, keepdims=True) + epsilon)
    unit_vec = output / magnitude
    return (preact, hidden, magnitude, unit_vec, unit_vec.astype(jnp.bfloat16))


def tower_backward(
    inputs, first_weight, second_weight, preact, hidden, magnitude, unit_vec, emb_gradient
):
    along = jnp.sum(unit_vec * emb_gradient, axis=-1, keepdims=True)
    out_gradient = ((emb_gradient - unit_vec * along) / magnitude).astype(jnp.bfloat16)
    second_grad = jnp.dot(hidden.T, out_gradient, preferred_element_type=jnp.float32)
    back_hidden = jnp.dot(out_gradient, second_weight.T, preferred_element_type=jnp.float32)
    hidden_grad = jnp.where(preact > 0, back_hidden, 0.0).astype(jnp.bfloat16)
    first_grad = jnp.dot(inputs.T, hidden_grad, preferred_element_type=jnp.float32)
    input_grad = jnp.dot(hidden_grad, first_weight.T, preferred_element_type=jnp.float32).astype(
        jnp.bfloat16
    )
    return (first_grad, second_grad, input_grad)


def onehot(index, count):
    return (index[:, None] == jnp.arange(count, dtype=jnp.int32)[None, :]).astype(jnp.bfloat16)


def gather_rows(table, index):
    picked = jnp.dot(onehot(index, table.shape[0]), table, preferred_element_type=jnp.float32)
    return picked.astype(jnp.bfloat16)


def scatter_rows(index, values, count):
    return lax.dot_general(
        onehot(index, count),
        values,
        (((0,), (0,)), ((), ())),
        preferred_element_type=jnp.float32,
    )


def pooled_input(fetched_rows, slot_flat, sample_count, emb_width):
    summed = scatter_rows(slot_flat, fetched_rows.reshape(-1, emb_width), sample_count * FEATS)
    return summed.astype(jnp.bfloat16).reshape(sample_count, FEATS * emb_width)


def per_device(
    user_table,
    item_table,
    user_pick,
    item_pick,
    user_slot,
    item_slot,
    user_w1,
    user_w2,
    item_w1,
    item_w2,
):
    shard_count = lax.axis_size("table")
    replica_count = lax.axis_size("dp")
    emb_width = user_table.shape[1]
    row_total = user_table.shape[0]
    item_rows = B_DEV + NEG_DEV
    cap_u = user_pick.shape[-1]
    cap_i = item_pick.shape[-1]
    user_picks = user_pick.reshape(-1)
    item_picks = item_pick.reshape(-1)
    user_slots = user_slot.reshape(-1)
    item_slots = item_slot.reshape(-1)
    user_fetch = gather_rows(user_table, user_picks).reshape(shard_count, cap_u, emb_width)
    item_fetch = gather_rows(item_table, item_picks).reshape(shard_count, cap_i, emb_width)
    fetched = lax.all_to_all(
        jnp.concatenate([user_fetch, item_fetch], axis=1),
        "table",
        split_axis=0,
        concat_axis=0,
        tiled=True,
    )
    user_fetched = fetched[:, :cap_u]
    item_fetched = fetched[:, cap_u:]
    user_input = pooled_input(user_fetched, user_slots, B_DEV, emb_width)
    user_state = tower_forward(user_input, user_w1, user_w2)
    item_input = pooled_input(item_fetched, item_slots, item_rows, emb_width)
    item_state = tower_forward(item_input, item_w1, item_w2)
    query_embedding_matrix = user_state[4]
    candidate_embedding_matrix = item_state[4]
    dp_index = lax.axis_index("dp")
    collected_rows = lax.all_gather(candidate_embedding_matrix, "dp", axis=0, tiled=True)
    pairwise_match_scores = (
        jnp.dot(query_embedding_matrix, collected_rows.T, preferred_element_type=jnp.float32)
        / score_divisor_scale
    )
    exponent = jnp.exp(pairwise_match_scores)
    learnable_model_state = exponent / jnp.sum(exponent, axis=1, keepdims=True)
    columns = jnp.arange(replica_count * item_rows, dtype=jnp.int32)
    positive = dp_index * item_rows + jnp.arange(B_DEV, dtype=jnp.int32)
    correct_class_indices = (columns[None, :] == positive[:, None]).astype(jnp.float32)
    score_derivative_matrix = (
        (learnable_model_state - correct_class_indices) / score_divisor_scale
    ).astype(jnp.bfloat16)
    user_emb_grad = jnp.dot(
        score_derivative_matrix, collected_rows, preferred_element_type=jnp.float32
    )
    item_emb_grad = lax.psum_scatter(
        lax.dot_general(
            score_derivative_matrix,
            query_embedding_matrix,
            (((0,), (0,)), ((), ())),
            preferred_element_type=jnp.float32,
        ),
        "dp",
        scatter_dimension=0,
        tiled=True,
    )
    user_back = tower_backward(
        user_input,
        user_w1,
        user_w2,
        user_state[0],
        user_state[1],
        user_state[2],
        user_state[3],
        user_emb_grad,
    )
    item_back = tower_backward(
        item_input,
        item_w1,
        item_w2,
        item_state[0],
        item_state[1],
        item_state[2],
        item_state[3],
        item_emb_grad,
    )
    weight_terms = (user_back[0], user_back[1], item_back[0], item_back[1])
    flat_terms = jnp.concatenate([t.reshape(-1) for t in weight_terms])
    device_total = shard_count * replica_count
    reduced = lax.psum_scatter(
        flat_terms.reshape(-1, 128), "dp", scatter_dimension=0, tiled=True
    )
    reduced = lax.optimization_barrier(lax.psum(reduced, "table"))
    gathered = lax.all_gather(
        reduced.astype(jnp.bfloat16), "dp", axis=0, tiled=True
    ).reshape(-1)
    weight_grads = []
    offset = 0
    for t in weight_terms:
        weight_grads.append(gathered[offset : offset + t.size].reshape(t.shape))
        offset += t.size
    user_grads = gather_rows(user_back[2].reshape(-1, emb_width), user_slots).reshape(
        shard_count, cap_u, emb_width
    )
    item_grads = gather_rows(item_back[2].reshape(-1, emb_width), item_slots).reshape(
        shard_count, cap_i, emb_width
    )
    arrived = lax.all_to_all(
        jnp.concatenate([user_grads, item_grads], axis=1),
        "table",
        split_axis=0,
        concat_axis=0,
        tiled=True,
    )
    user_total = scatter_rows(user_picks, arrived[:, :cap_u].reshape(-1, emb_width), row_total)
    item_total = scatter_rows(item_picks, arrived[:, cap_u:].reshape(-1, emb_width), row_total)
    user_table_grad, item_table_grad = (
        lax.psum_scatter(user_total, "dp", scatter_dimension=0, tiled=True),
        lax.psum_scatter(item_total, "dp", scatter_dimension=0, tiled=True),
    )
    return (
        user_table_grad,
        item_table_grad,
        weight_grads[0],
        weight_grads[1],
        weight_grads[2],
        weight_grads[3],
    )


def solution(mesh):
    in_specs = (
        P("table", None),
        P("table", None),
        P("table", "dp", None, None),
        P("table", "dp", None, None),
        P("table", "dp", None, None),
        P("table", "dp", None, None),
        P(),
        P(),
        P(),
        P(),
    )
    out_specs = (P(("table", "dp"), None), P(("table", "dp"), None), P(), P(), P(), P())
    return jax.shard_map(
        per_device, mesh=mesh, in_specs=in_specs, out_specs=out_specs, check_vma=False
    )
```

```python
import jax
import jax.numpy as jnp
from jax import lax
from jax.sharding import PartitionSpec as P

FEATS = 2
B_DEV = 128
NEG_DEV = 32


score_divisor_scale = 0.05
epsilon = 1e-06


def tower_forward(inputs, first_weight, second_weight):
    preact = jnp.dot(inputs, first_weight, preferred_element_type=jnp.float32)
    hidden = jnp.maximum(preact, 0.0).astype(jnp.bfloat16)
    output = jnp.dot(hidden, second_weight, preferred_element_type=jnp.float32)
    magnitude = jnp.sqrt(jnp.sum(output * output, axis=-1, keepdims=True) + epsilon)
    unit_vec = output / magnitude
    return (preact, hidden, magnitude, unit_vec, unit_vec.astype(jnp.bfloat16))


def tower_backward(
    inputs, first_weight, second_weight, preact, hidden, magnitude, unit_vec, emb_gradient
):
    along = jnp.sum(unit_vec * emb_gradient, axis=-1, keepdims=True)
    out_gradient = ((emb_gradient - unit_vec * along) / magnitude).astype(jnp.bfloat16)
    second_grad = jnp.dot(hidden.T, out_gradient, preferred_element_type=jnp.float32)
    back_hidden = jnp.dot(out_gradient, second_weight.T, preferred_element_type=jnp.float32)
    hidden_grad = jnp.where(preact > 0, back_hidden, 0.0).astype(jnp.bfloat16)
    first_grad = jnp.dot(inputs.T, hidden_grad, preferred_element_type=jnp.float32)
    input_grad = jnp.dot(hidden_grad, first_weight.T, preferred_element_type=jnp.float32).astype(
        jnp.bfloat16
    )
    return (first_grad, second_grad, input_grad)


def onehot(index, count):
    return (index[:, None] == jnp.arange(count, dtype=jnp.int32)[None, :]).astype(jnp.bfloat16)


def gather_rows(table, index):
    picked = jnp.dot(onehot(index, table.shape[0]), table, preferred_element_type=jnp.float32)
    return picked.astype(jnp.bfloat16)


def scatter_rows(index, values, count):
    return lax.dot_general(
        onehot(index, count),
        values,
        (((0,), (0,)), ((), ())),
        preferred_element_type=jnp.float32,
    )


def pooled_input(fetched_rows, slot_flat, sample_count, emb_width):
    summed = scatter_rows(slot_flat, fetched_rows.reshape(-1, emb_width), sample_count * FEATS)
    return summed.astype(jnp.bfloat16).reshape(sample_count, FEATS * emb_width)


def per_device(
    user_table,
    item_table,
    user_pick,
    item_pick,
    user_slot,
    item_slot,
    user_w1,
    user_w2,
    item_w1,
    item_w2,
):
    shard_count = lax.axis_size("table")
    replica_count = lax.axis_size("dp")
    emb_width = user_table.shape[1]
    row_total = user_table.shape[0]
    item_rows = B_DEV + NEG_DEV
    cap_u = user_pick.shape[-1]
    cap_i = item_pick.shape[-1]
    user_picks = user_pick.reshape(-1)
    item_picks = item_pick.reshape(-1)
    user_slots = user_slot.reshape(-1)
    item_slots = item_slot.reshape(-1)
    user_fetch = gather_rows(user_table, user_picks).reshape(shard_count, cap_u, emb_width)
    item_fetch = gather_rows(item_table, item_picks).reshape(shard_count, cap_i, emb_width)
    fetched = lax.all_to_all(
        jnp.concatenate([user_fetch, item_fetch], axis=1),
        "table",
        split_axis=0,
        concat_axis=0,
        tiled=True,
    )
    user_fetched = fetched[:, :cap_u]
    item_fetched = fetched[:, cap_u:]
    user_input = pooled_input(user_fetched, user_slots, B_DEV, emb_width)
    user_state = tower_forward(user_input, user_w1, user_w2)
    item_input = pooled_input(item_fetched, item_slots, item_rows, emb_width)
    item_state = tower_forward(item_input, item_w1, item_w2)
    query_embedding_matrix = user_state[4]
    candidate_embedding_matrix = item_state[4]
    dp_index = lax.axis_index("dp")
    collected = lax.all_gather(
        jnp.concatenate([query_embedding_matrix, candidate_embedding_matrix], axis=0),
        "dp",
        axis=0,
    )
    group_users = collected[:, :B_DEV].reshape(-1, emb_width)
    collected_rows = collected[:, B_DEV:].reshape(-1, emb_width)
    pairwise_match_scores = (
        jnp.dot(group_users, collected_rows.T, preferred_element_type=jnp.float32)
        / score_divisor_scale
    )
    exponent = jnp.exp(pairwise_match_scores)
    learnable_model_state = exponent / jnp.sum(exponent, axis=1, keepdims=True)
    columns = jnp.arange(replica_count * item_rows, dtype=jnp.int32)
    user_index = jnp.arange(replica_count * B_DEV, dtype=jnp.int32)
    positive = user_index // B_DEV * item_rows + user_index % B_DEV
    correct_class_indices = (columns[None, :] == positive[:, None]).astype(jnp.float32)
    score_derivative_matrix = (
        (learnable_model_state - correct_class_indices) / score_divisor_scale
    ).astype(jnp.bfloat16)
    own_rows = lax.dynamic_slice_in_dim(score_derivative_matrix, dp_index * B_DEV, B_DEV, axis=0)
    own_columns = lax.dynamic_slice_in_dim(
        score_derivative_matrix, dp_index * item_rows, item_rows, axis=1
    )
    user_emb_grad = jnp.dot(own_rows, collected_rows, preferred_element_type=jnp.float32)
    item_emb_grad = lax.dot_general(
        own_columns,
        group_users,
        (((0,), (0,)), ((), ())),
        preferred_element_type=jnp.float32,
    )
    user_back = tower_backward(
        user_input,
        user_w1,
        user_w2,
        user_state[0],
        user_state[1],
        user_state[2],
        user_state[3],
        user_emb_grad,
    )
    item_back = tower_backward(
        item_input,
        item_w1,
        item_w2,
        item_state[0],
        item_state[1],
        item_state[2],
        item_state[3],
        item_emb_grad,
    )
    weight_grads = [
        g.astype(jnp.bfloat16)
        for g in lax.psum((user_back[0], user_back[1], item_back[0], item_back[1]), ("table", "dp"))
    ]
    user_grads = gather_rows(user_back[2].reshape(-1, emb_width), user_slots).reshape(
        shard_count, cap_u, emb_width
    )
    item_grads = gather_rows(item_back[2].reshape(-1, emb_width), item_slots).reshape(
        shard_count, cap_i, emb_width
    )
    arrived = lax.all_to_all(
        jnp.concatenate([user_grads, item_grads], axis=1),
        "table",
        split_axis=0,
        concat_axis=0,
        tiled=True,
    )
    user_total = scatter_rows(user_picks, arrived[:, :cap_u].reshape(-1, emb_width), row_total)
    item_total = scatter_rows(item_picks, arrived[:, cap_u:].reshape(-1, emb_width), row_total)
    both_totals = jnp.stack(
        [
            user_total.reshape(replica_count, -1, emb_width),
            item_total.reshape(replica_count, -1, emb_width),
        ],
        axis=1,
    ).reshape(-1, emb_width)
    both_grads = lax.psum_scatter(both_totals, "dp", scatter_dimension=0, tiled=True)
    user_table_grad, item_table_grad = jnp.split(both_grads, 2, axis=0)
    return (
        user_table_grad,
        item_table_grad,
        weight_grads[0],
        weight_grads[1],
        weight_grads[2],
        weight_grads[3],
    )


def solution(mesh):
    in_specs = (
        P("table", None),
        P("table", None),
        P("table", "dp", None, None),
        P("table", "dp", None, None),
        P("table", "dp", None, None),
        P("table", "dp", None, None),
        P(),
        P(),
        P(),
        P(),
    )
    out_specs = (P(("table", "dp"), None), P(("table", "dp"), None), P(), P(), P(), P())
    return jax.shard_map(
        per_device, mesh=mesh, in_specs=in_specs, out_specs=out_specs, check_vma=False
    )
```

```python
import jax
import jax.numpy as jnp
from jax import lax
from jax.sharding import PartitionSpec as P

FEATS = 2
B_DEV = 128
NEG_DEV = 32


score_divisor_scale = 0.05
epsilon = 1e-06


def tower_forward(inputs, first_weight, second_weight):
    preact = jnp.dot(inputs, first_weight, preferred_element_type=jnp.float32)
    hidden = jnp.maximum(preact, 0.0).astype(jnp.bfloat16)
    output = jnp.dot(hidden, second_weight, preferred_element_type=jnp.float32)
    magnitude = jnp.sqrt(jnp.sum(output * output, axis=-1, keepdims=True) + epsilon)
    unit_vec = output / magnitude
    return (preact, hidden, magnitude, unit_vec, unit_vec.astype(jnp.bfloat16))


def tower_backward(
    inputs, first_weight, second_weight, preact, hidden, magnitude, unit_vec, emb_gradient
):
    along = jnp.sum(unit_vec * emb_gradient, axis=-1, keepdims=True)
    out_gradient = ((emb_gradient - unit_vec * along) / magnitude).astype(jnp.bfloat16)
    second_grad = jnp.dot(hidden.T, out_gradient, preferred_element_type=jnp.float32)
    back_hidden = jnp.dot(out_gradient, second_weight.T, preferred_element_type=jnp.float32)
    hidden_grad = jnp.where(preact > 0, back_hidden, 0.0).astype(jnp.bfloat16)
    first_grad = jnp.dot(inputs.T, hidden_grad, preferred_element_type=jnp.float32)
    input_grad = jnp.dot(hidden_grad, first_weight.T, preferred_element_type=jnp.float32).astype(
        jnp.bfloat16
    )
    return (first_grad, second_grad, input_grad)


def onehot(index, count):
    return (index[:, None] == jnp.arange(count, dtype=jnp.int32)[None, :]).astype(jnp.bfloat16)


def gather_rows(table, index):
    picked = jnp.dot(onehot(index, table.shape[0]), table, preferred_element_type=jnp.float32)
    return picked.astype(jnp.bfloat16)


def scatter_rows(index, values, count):
    return lax.dot_general(
        onehot(index, count),
        values,
        (((0,), (0,)), ((), ())),
        preferred_element_type=jnp.float32,
    )


def pooled_input(fetched_rows, slot_flat, sample_count, emb_width):
    summed = scatter_rows(slot_flat, fetched_rows.reshape(-1, emb_width), sample_count * FEATS)
    return summed.astype(jnp.bfloat16).reshape(sample_count, FEATS * emb_width)


def per_device(
    user_table,
    item_table,
    user_pick,
    item_pick,
    user_slot,
    item_slot,
    user_w1,
    user_w2,
    item_w1,
    item_w2,
):
    shard_count = lax.axis_size("table")
    replica_count = lax.axis_size("dp")
    emb_width = user_table.shape[1]
    row_total = user_table.shape[0]
    item_rows = B_DEV + NEG_DEV
    cap_u = user_pick.shape[-1]
    cap_i = item_pick.shape[-1]
    user_picks = user_pick.reshape(-1)
    item_picks = item_pick.reshape(-1)
    user_slots = user_slot.reshape(-1)
    item_slots = item_slot.reshape(-1)
    user_fetch = gather_rows(user_table, user_picks).reshape(shard_count, cap_u, emb_width)
    item_fetch = gather_rows(item_table, item_picks).reshape(shard_count, cap_i, emb_width)
    fetched = lax.all_to_all(
        jnp.concatenate([user_fetch, item_fetch], axis=1),
        "table",
        split_axis=0,
        concat_axis=0,
        tiled=True,
    )
    user_fetched = fetched[:, :cap_u]
    item_fetched = fetched[:, cap_u:]
    user_input = pooled_input(user_fetched, user_slots, B_DEV, emb_width)
    user_state = tower_forward(user_input, user_w1, user_w2)
    item_input = pooled_input(item_fetched, item_slots, item_rows, emb_width)
    item_state = tower_forward(item_input, item_w1, item_w2)
    query_embedding_matrix = user_state[4]
    candidate_embedding_matrix = item_state[4]
    dp_index = lax.axis_index("dp")
    collected = lax.all_gather(
        jnp.concatenate([query_embedding_matrix, candidate_embedding_matrix], axis=0),
        "dp",
        axis=0,
    )
    group_users = collected[:, :B_DEV].reshape(-1, emb_width)
    collected_rows = collected[:, B_DEV:].reshape(-1, emb_width)
    pairwise_match_scores = (
        jnp.dot(group_users, collected_rows.T, preferred_element_type=jnp.float32)
        / score_divisor_scale
    )
    exponent = jnp.exp(pairwise_match_scores)
    learnable_model_state = exponent / jnp.sum(exponent, axis=1, keepdims=True)
    columns = jnp.arange(replica_count * item_rows, dtype=jnp.int32)
    user_index = jnp.arange(replica_count * B_DEV, dtype=jnp.int32)
    positive = user_index // B_DEV * item_rows + user_index % B_DEV
    correct_class_indices = (columns[None, :] == positive[:, None]).astype(jnp.float32)
    score_derivative_matrix = (
        (learnable_model_state - correct_class_indices) / score_divisor_scale
    ).astype(jnp.bfloat16)
    own_rows = lax.dynamic_slice_in_dim(score_derivative_matrix, dp_index * B_DEV, B_DEV, axis=0)
    own_columns = lax.dynamic_slice_in_dim(
        score_derivative_matrix, dp_index * item_rows, item_rows, axis=1
    )
    user_emb_grad = jnp.dot(own_rows, collected_rows, preferred_element_type=jnp.float32)
    item_emb_grad = lax.dot_general(
        own_columns,
        group_users,
        (((0,), (0,)), ((), ())),
        preferred_element_type=jnp.float32,
    )
    user_back = tower_backward(
        user_input,
        user_w1,
        user_w2,
        user_state[0],
        user_state[1],
        user_state[2],
        user_state[3],
        user_emb_grad,
    )
    item_back = tower_backward(
        item_input,
        item_w1,
        item_w2,
        item_state[0],
        item_state[1],
        item_state[2],
        item_state[3],
        item_emb_grad,
    )
    weight_terms = (user_back[0], user_back[1], item_back[0], item_back[1])
    flat_terms = jnp.concatenate([t.reshape(-1) for t in weight_terms])
    flat_sum = lax.optimization_barrier(lax.psum(flat_terms, ("table", "dp")))
    flat_grads = flat_sum.astype(jnp.bfloat16)
    weight_grads = []
    offset = 0
    for t in weight_terms:
        weight_grads.append(flat_grads[offset : offset + t.size].reshape(t.shape))
        offset += t.size
    user_grads = gather_rows(user_back[2].reshape(-1, emb_width), user_slots).reshape(
        shard_count, cap_u, emb_width
    )
    item_grads = gather_rows(item_back[2].reshape(-1, emb_width), item_slots).reshape(
        shard_count, cap_i, emb_width
    )
    arrived = lax.all_to_all(
        jnp.concatenate([user_grads, item_grads], axis=1),
        "table",
        split_axis=0,
        concat_axis=0,
        tiled=True,
    )
    user_total = scatter_rows(user_picks, arrived[:, :cap_u].reshape(-1, emb_width), row_total)
    item_total = scatter_rows(item_picks, arrived[:, cap_u:].reshape(-1, emb_width), row_total)
    both_totals = jnp.stack(
        [
            user_total.reshape(replica_count, -1, emb_width),
            item_total.reshape(replica_count, -1, emb_width),
        ],
        axis=1,
    ).reshape(-1, emb_width)
    both_parts = lax.all_to_all(
        both_totals.reshape(replica_count, -1, emb_width), "dp", 0, 0, tiled=True
    )
    both_grads = jnp.sum(both_parts, axis=0)
    user_table_grad, item_table_grad = jnp.split(both_grads, 2, axis=0)
    return (
        user_table_grad,
        item_table_grad,
        weight_grads[0],
        weight_grads[1],
        weight_grads[2],
        weight_grads[3],
    )


def solution(mesh):
    in_specs = (
        P("table", None),
        P("table", None),
        P("table", "dp", None, None),
        P("table", "dp", None, None),
        P("table", "dp", None, None),
        P("table", "dp", None, None),
        P(),
        P(),
        P(),
        P(),
    )
    out_specs = (P(("table", "dp"), None), P(("table", "dp"), None), P(), P(), P(), P())
    return jax.shard_map(
        per_device, mesh=mesh, in_specs=in_specs, out_specs=out_specs, check_vma=False
    )
```

```python
import jax
import jax.numpy as jnp
from jax import lax
from jax.sharding import PartitionSpec as P

FEATS = 2
B_DEV = 128
NEG_DEV = 32


score_divisor_scale = 0.05
epsilon = 1e-06


def tower_forward(inputs, first_weight, second_weight):
    preact = jnp.dot(inputs, first_weight, preferred_element_type=jnp.float32)
    hidden = jnp.maximum(preact, 0.0).astype(jnp.bfloat16)
    output = jnp.dot(hidden, second_weight, preferred_element_type=jnp.float32)
    magnitude = jnp.sqrt(jnp.sum(output * output, axis=-1, keepdims=True) + epsilon)
    unit_vec = output / magnitude
    return (preact, hidden, magnitude, unit_vec, unit_vec.astype(jnp.bfloat16))


def tower_backward(
    inputs, first_weight, second_weight, preact, hidden, magnitude, unit_vec, emb_gradient
):
    along = jnp.sum(unit_vec * emb_gradient, axis=-1, keepdims=True)
    out_gradient = ((emb_gradient - unit_vec * along) / magnitude).astype(jnp.bfloat16)
    second_grad = jnp.dot(hidden.T, out_gradient, preferred_element_type=jnp.float32)
    back_hidden = jnp.dot(out_gradient, second_weight.T, preferred_element_type=jnp.float32)
    hidden_grad = jnp.where(preact > 0, back_hidden, 0.0).astype(jnp.bfloat16)
    first_grad = jnp.dot(inputs.T, hidden_grad, preferred_element_type=jnp.float32)
    input_grad = jnp.dot(hidden_grad, first_weight.T, preferred_element_type=jnp.float32).astype(
        jnp.bfloat16
    )
    return (first_grad, second_grad, input_grad)


def onehot(index, count):
    return (index[:, None] == jnp.arange(count, dtype=jnp.int32)[None, :]).astype(jnp.bfloat16)


def gather_rows(table, index):
    picked = jnp.dot(onehot(index, table.shape[0]), table, preferred_element_type=jnp.float32)
    return picked.astype(jnp.bfloat16)


def scatter_rows(index, values, count):
    return lax.dot_general(
        onehot(index, count),
        values,
        (((0,), (0,)), ((), ())),
        preferred_element_type=jnp.float32,
    )


def pooled_input(fetched_rows, slot_flat, sample_count, emb_width):
    summed = scatter_rows(slot_flat, fetched_rows.reshape(-1, emb_width), sample_count * FEATS)
    return summed.astype(jnp.bfloat16).reshape(sample_count, FEATS * emb_width)


def per_device(
    user_table,
    item_table,
    user_pick,
    item_pick,
    user_slot,
    item_slot,
    user_w1,
    user_w2,
    item_w1,
    item_w2,
):
    shard_count = lax.axis_size("table")
    replica_count = lax.axis_size("dp")
    emb_width = user_table.shape[1]
    row_total = user_table.shape[0]
    item_rows = B_DEV + NEG_DEV
    cap_u = user_pick.shape[-1]
    cap_i = item_pick.shape[-1]
    user_picks = user_pick.reshape(-1)
    item_picks = item_pick.reshape(-1)
    user_slots = user_slot.reshape(-1)
    item_slots = item_slot.reshape(-1)
    user_fetch = gather_rows(user_table, user_picks).reshape(shard_count, cap_u, emb_width)
    item_fetch = gather_rows(item_table, item_picks).reshape(shard_count, cap_i, emb_width)
    fetched = lax.all_to_all(
        jnp.concatenate([user_fetch, item_fetch], axis=1),
        "table",
        split_axis=0,
        concat_axis=0,
        tiled=True,
    )
    user_fetched = fetched[:, :cap_u]
    item_fetched = fetched[:, cap_u:]
    user_input = pooled_input(user_fetched, user_slots, B_DEV, emb_width)
    user_state = tower_forward(user_input, user_w1, user_w2)
    item_input = pooled_input(item_fetched, item_slots, item_rows, emb_width)
    item_state = tower_forward(item_input, item_w1, item_w2)
    query_embedding_matrix = user_state[4]
    candidate_embedding_matrix = item_state[4]
    dp_index = lax.axis_index("dp")
    collected = lax.all_gather(
        jnp.concatenate([query_embedding_matrix, candidate_embedding_matrix], axis=0),
        "dp",
        axis=0,
    )
    group_users = collected[:, :B_DEV].reshape(-1, emb_width)
    collected_rows = collected[:, B_DEV:].reshape(-1, emb_width)
    pairwise_match_scores = (
        jnp.dot(group_users, collected_rows.T, preferred_element_type=jnp.float32)
        / score_divisor_scale
    )
    exponent = jnp.exp(pairwise_match_scores)
    learnable_model_state = exponent / jnp.sum(exponent, axis=1, keepdims=True)
    columns = jnp.arange(replica_count * item_rows, dtype=jnp.int32)
    user_index = jnp.arange(replica_count * B_DEV, dtype=jnp.int32)
    positive = user_index // B_DEV * item_rows + user_index % B_DEV
    correct_class_indices = (columns[None, :] == positive[:, None]).astype(jnp.float32)
    score_derivative_matrix = (
        (learnable_model_state - correct_class_indices) / score_divisor_scale
    ).astype(jnp.bfloat16)
    own_rows = lax.dynamic_slice_in_dim(score_derivative_matrix, dp_index * B_DEV, B_DEV, axis=0)
    own_columns = lax.dynamic_slice_in_dim(
        score_derivative_matrix, dp_index * item_rows, item_rows, axis=1
    )
    user_emb_grad = jnp.dot(own_rows, collected_rows, preferred_element_type=jnp.float32)
    item_emb_grad = lax.dot_general(
        own_columns,
        group_users,
        (((0,), (0,)), ((), ())),
        preferred_element_type=jnp.float32,
    )
    user_back = tower_backward(
        user_input,
        user_w1,
        user_w2,
        user_state[0],
        user_state[1],
        user_state[2],
        user_state[3],
        user_emb_grad,
    )
    item_back = tower_backward(
        item_input,
        item_w1,
        item_w2,
        item_state[0],
        item_state[1],
        item_state[2],
        item_state[3],
        item_emb_grad,
    )
    user_grads = gather_rows(user_back[2].reshape(-1, emb_width), user_slots).reshape(
        shard_count, cap_u, emb_width
    )
    item_grads = gather_rows(item_back[2].reshape(-1, emb_width), item_slots).reshape(
        shard_count, cap_i, emb_width
    )
    slot_grads = jnp.concatenate([user_grads, item_grads], axis=1)
    user_flat, slot_grads = lax.optimization_barrier(
        (jnp.concatenate([user_back[0].reshape(-1), user_back[1].reshape(-1)]), slot_grads)
    )
    user_sum = lax.optimization_barrier(lax.psum(user_flat, ("table", "dp")))
    arrived = lax.all_to_all(
        slot_grads,
        "table",
        split_axis=0,
        concat_axis=0,
        tiled=True,
    )
    user_total = scatter_rows(user_picks, arrived[:, :cap_u].reshape(-1, emb_width), row_total)
    item_total = scatter_rows(item_picks, arrived[:, cap_u:].reshape(-1, emb_width), row_total)
    both_totals = jnp.stack(
        [
            user_total.reshape(replica_count, -1, emb_width),
            item_total.reshape(replica_count, -1, emb_width),
        ],
        axis=1,
    ).reshape(-1, emb_width)
    item_flat, both_totals, user_sum = lax.optimization_barrier(
        (
            jnp.concatenate([item_back[0].reshape(-1), item_back[1].reshape(-1)]),
            both_totals,
            user_sum,
        )
    )
    item_sum = lax.optimization_barrier(lax.psum(item_flat, ("table", "dp")))
    both_parts = lax.all_to_all(
        both_totals.reshape(replica_count, -1, emb_width), "dp", 0, 0, tiled=True
    )
    weight_grads = []
    for flat_sum, tower_terms in (
        (user_sum, (user_back[0], user_back[1])),
        (item_sum, (item_back[0], item_back[1])),
    ):
        flat_grads = flat_sum.astype(jnp.bfloat16)
        offset = 0
        for t in tower_terms:
            weight_grads.append(flat_grads[offset : offset + t.size].reshape(t.shape))
            offset += t.size
    both_grads = jnp.sum(both_parts, axis=0)
    user_table_grad, item_table_grad = jnp.split(both_grads, 2, axis=0)
    return (
        user_table_grad,
        item_table_grad,
        weight_grads[0],
        weight_grads[1],
        weight_grads[2],
        weight_grads[3],
    )


def solution(mesh):
    in_specs = (
        P("table", None),
        P("table", None),
        P("table", "dp", None, None),
        P("table", "dp", None, None),
        P("table", "dp", None, None),
        P("table", "dp", None, None),
        P(),
        P(),
        P(),
        P(),
    )
    out_specs = (P(("table", "dp"), None), P(("table", "dp"), None), P(), P(), P(), P())
    return jax.shard_map(
        per_device, mesh=mesh, in_specs=in_specs, out_specs=out_specs, check_vma=False
    )
```

```python
import jax
import jax.numpy as jnp
from jax import lax
from jax.sharding import PartitionSpec as P

FEATS = 2
B_DEV = 128
NEG_DEV = 32


score_divisor_scale = 0.05
epsilon = 1e-06


def tower_forward(inputs, first_weight, second_weight):
    preact = jnp.dot(inputs, first_weight, preferred_element_type=jnp.float32)
    hidden = jnp.maximum(preact, 0.0).astype(jnp.bfloat16)
    output = jnp.dot(hidden, second_weight, preferred_element_type=jnp.float32)
    magnitude = jnp.sqrt(jnp.sum(output * output, axis=-1, keepdims=True) + epsilon)
    unit_vec = output / magnitude
    return (preact, hidden, magnitude, unit_vec, unit_vec.astype(jnp.bfloat16))


def tower_backward(
    inputs, first_weight, second_weight, preact, hidden, magnitude, unit_vec, emb_gradient
):
    along = jnp.sum(unit_vec * emb_gradient, axis=-1, keepdims=True)
    out_gradient = ((emb_gradient - unit_vec * along) / magnitude).astype(jnp.bfloat16)
    second_grad = jnp.dot(hidden.T, out_gradient, preferred_element_type=jnp.float32)
    back_hidden = jnp.dot(out_gradient, second_weight.T, preferred_element_type=jnp.float32)
    hidden_grad = jnp.where(preact > 0, back_hidden, 0.0).astype(jnp.bfloat16)
    first_grad = jnp.dot(inputs.T, hidden_grad, preferred_element_type=jnp.float32)
    input_grad = jnp.dot(hidden_grad, first_weight.T, preferred_element_type=jnp.float32).astype(
        jnp.bfloat16
    )
    return (first_grad, second_grad, input_grad)


def onehot(index, count):
    return (index[:, None] == jnp.arange(count, dtype=jnp.int32)[None, :]).astype(jnp.bfloat16)


def gather_rows(table, index):
    picked = jnp.dot(onehot(index, table.shape[0]), table, preferred_element_type=jnp.float32)
    return picked.astype(jnp.bfloat16)


def scatter_rows(index, values, count):
    return lax.dot_general(
        onehot(index, count),
        values,
        (((0,), (0,)), ((), ())),
        preferred_element_type=jnp.float32,
    )


def pooled_input(fetched_rows, slot_flat, sample_count, emb_width):
    summed = scatter_rows(slot_flat, fetched_rows.reshape(-1, emb_width), sample_count * FEATS)
    return summed.astype(jnp.bfloat16).reshape(sample_count, FEATS * emb_width)


def per_device(
    user_table,
    item_table,
    user_pick,
    item_pick,
    user_slot,
    item_slot,
    user_w1,
    user_w2,
    item_w1,
    item_w2,
):
    shard_count = lax.axis_size("table")
    replica_count = lax.axis_size("dp")
    emb_width = user_table.shape[1]
    row_total = user_table.shape[0]
    item_rows = B_DEV + NEG_DEV
    cap_u = user_pick.shape[-1]
    cap_i = item_pick.shape[-1]
    user_picks = user_pick.reshape(-1)
    item_picks = item_pick.reshape(-1)
    user_slots = user_slot.reshape(-1)
    item_slots = item_slot.reshape(-1)
    user_fetch = gather_rows(user_table, user_picks).reshape(shard_count, cap_u, emb_width)
    item_fetch = gather_rows(item_table, item_picks).reshape(shard_count, cap_i, emb_width)
    fetched = lax.all_to_all(
        jnp.concatenate([user_fetch, item_fetch], axis=1),
        "table",
        split_axis=0,
        concat_axis=0,
        tiled=True,
    )
    user_fetched = fetched[:, :cap_u]
    item_fetched = fetched[:, cap_u:]
    user_input = pooled_input(user_fetched, user_slots, B_DEV, emb_width)
    user_state = tower_forward(user_input, user_w1, user_w2)
    item_input = pooled_input(item_fetched, item_slots, item_rows, emb_width)
    item_state = tower_forward(item_input, item_w1, item_w2)
    query_embedding_matrix = user_state[4]
    candidate_embedding_matrix = item_state[4]
    dp_index = lax.axis_index("dp")
    own_block = jnp.concatenate([query_embedding_matrix, candidate_embedding_matrix], axis=0)
    collected = lax.all_to_all(
        jnp.broadcast_to(own_block[None], (replica_count,) + own_block.shape), "dp", 0, 0
    )
    group_users = collected[:, :B_DEV].reshape(-1, emb_width)
    collected_rows = collected[:, B_DEV:].reshape(-1, emb_width)
    pairwise_match_scores = (
        jnp.dot(group_users, collected_rows.T, preferred_element_type=jnp.float32)
        / score_divisor_scale
    )
    exponent = jnp.exp(pairwise_match_scores)
    learnable_model_state = exponent / jnp.sum(exponent, axis=1, keepdims=True)
    columns = jnp.arange(replica_count * item_rows, dtype=jnp.int32)
    user_index = jnp.arange(replica_count * B_DEV, dtype=jnp.int32)
    positive = user_index // B_DEV * item_rows + user_index % B_DEV
    correct_class_indices = (columns[None, :] == positive[:, None]).astype(jnp.float32)
    score_derivative_matrix = (
        (learnable_model_state - correct_class_indices) / score_divisor_scale
    ).astype(jnp.bfloat16)
    own_rows = lax.dynamic_slice_in_dim(score_derivative_matrix, dp_index * B_DEV, B_DEV, axis=0)
    own_columns = lax.dynamic_slice_in_dim(
        score_derivative_matrix, dp_index * item_rows, item_rows, axis=1
    )
    user_emb_grad = jnp.dot(own_rows, collected_rows, preferred_element_type=jnp.float32)
    item_emb_grad = lax.dot_general(
        own_columns,
        group_users,
        (((0,), (0,)), ((), ())),
        preferred_element_type=jnp.float32,
    )
    user_back = tower_backward(
        user_input,
        user_w1,
        user_w2,
        user_state[0],
        user_state[1],
        user_state[2],
        user_state[3],
        user_emb_grad,
    )
    item_back = tower_backward(
        item_input,
        item_w1,
        item_w2,
        item_state[0],
        item_state[1],
        item_state[2],
        item_state[3],
        item_emb_grad,
    )
    weight_terms = (user_back[0], user_back[1], item_back[0], item_back[1])
    flat_terms = jnp.concatenate([t.reshape(-1) for t in weight_terms])
    flat_sum = lax.optimization_barrier(lax.psum(flat_terms, ("table", "dp")))
    flat_grads = flat_sum.astype(jnp.bfloat16)
    weight_grads = []
    offset = 0
    for t in weight_terms:
        weight_grads.append(flat_grads[offset : offset + t.size].reshape(t.shape))
        offset += t.size
    user_grads = gather_rows(user_back[2].reshape(-1, emb_width), user_slots).reshape(
        shard_count, cap_u, emb_width
    )
    item_grads = gather_rows(item_back[2].reshape(-1, emb_width), item_slots).reshape(
        shard_count, cap_i, emb_width
    )
    arrived = lax.all_to_all(
        jnp.concatenate([user_grads, item_grads], axis=1),
        "table",
        split_axis=0,
        concat_axis=0,
        tiled=True,
    )
    user_total = scatter_rows(user_picks, arrived[:, :cap_u].reshape(-1, emb_width), row_total)
    item_total = scatter_rows(item_picks, arrived[:, cap_u:].reshape(-1, emb_width), row_total)
    both_totals = jnp.stack(
        [
            user_total.reshape(replica_count, -1, emb_width),
            item_total.reshape(replica_count, -1, emb_width),
        ],
        axis=1,
    ).reshape(-1, emb_width)
    both_parts = lax.all_to_all(
        both_totals.reshape(replica_count, -1, emb_width), "dp", 0, 0, tiled=True
    )
    both_grads = jnp.sum(both_parts, axis=0)
    user_table_grad, item_table_grad = jnp.split(both_grads, 2, axis=0)
    return (
        user_table_grad,
        item_table_grad,
        weight_grads[0],
        weight_grads[1],
        weight_grads[2],
        weight_grads[3],
    )


def solution(mesh):
    in_specs = (
        P("table", None),
        P("table", None),
        P("table", "dp", None, None),
        P("table", "dp", None, None),
        P("table", "dp", None, None),
        P("table", "dp", None, None),
        P(),
        P(),
        P(),
        P(),
    )
    out_specs = (P(("table", "dp"), None), P(("table", "dp"), None), P(), P(), P(), P())
    return jax.shard_map(
        per_device, mesh=mesh, in_specs=in_specs, out_specs=out_specs, check_vma=False
    )
```

```python
import jax
import jax.numpy as jnp
from jax import lax
from jax.sharding import PartitionSpec as P

FEATS = 2
B_DEV = 128
NEG_DEV = 32


score_divisor_scale = 0.05
epsilon = 1e-06


def tower_forward(inputs, first_weight, second_weight):
    preact = jnp.dot(inputs, first_weight, preferred_element_type=jnp.float32)
    hidden = jnp.maximum(preact, 0.0).astype(jnp.bfloat16)
    output = jnp.dot(hidden, second_weight, preferred_element_type=jnp.float32)
    magnitude = jnp.sqrt(jnp.sum(output * output, axis=-1, keepdims=True) + epsilon)
    unit_vec = output / magnitude
    return (preact, hidden, magnitude, unit_vec, unit_vec.astype(jnp.bfloat16))


def tower_backward(
    inputs, first_weight, second_weight, preact, hidden, magnitude, unit_vec, emb_gradient
):
    along = jnp.sum(unit_vec * emb_gradient, axis=-1, keepdims=True)
    out_gradient = ((emb_gradient - unit_vec * along) / magnitude).astype(jnp.bfloat16)
    second_grad = jnp.dot(hidden.T, out_gradient, preferred_element_type=jnp.float32)
    back_hidden = jnp.dot(out_gradient, second_weight.T, preferred_element_type=jnp.float32)
    hidden_grad = jnp.where(preact > 0, back_hidden, 0.0).astype(jnp.bfloat16)
    first_grad = jnp.dot(inputs.T, hidden_grad, preferred_element_type=jnp.float32)
    input_grad = jnp.dot(hidden_grad, first_weight.T, preferred_element_type=jnp.float32).astype(
        jnp.bfloat16
    )
    return (first_grad, second_grad, input_grad)


def onehot(index, count):
    return (index[:, None] == jnp.arange(count, dtype=jnp.int32)[None, :]).astype(jnp.bfloat16)


def gather_rows(table, index):
    picked = jnp.dot(onehot(index, table.shape[0]), table, preferred_element_type=jnp.float32)
    return picked.astype(jnp.bfloat16)


def scatter_rows(index, values, count):
    return lax.dot_general(
        onehot(index, count),
        values,
        (((0,), (0,)), ((), ())),
        preferred_element_type=jnp.float32,
    )


def pooled_input(fetched_rows, slot_flat, sample_count, emb_width):
    summed = scatter_rows(slot_flat, fetched_rows.reshape(-1, emb_width), sample_count * FEATS)
    return summed.astype(jnp.bfloat16).reshape(sample_count, FEATS * emb_width)


def per_device(
    user_table,
    item_table,
    user_pick,
    item_pick,
    user_slot,
    item_slot,
    user_w1,
    user_w2,
    item_w1,
    item_w2,
):
    shard_count = lax.axis_size("table")
    replica_count = lax.axis_size("dp")
    emb_width = user_table.shape[1]
    row_total = user_table.shape[0]
    item_rows = B_DEV + NEG_DEV
    cap_u = user_pick.shape[-1]
    cap_i = item_pick.shape[-1]
    user_picks = user_pick.reshape(-1)
    item_picks = item_pick.reshape(-1)
    user_slots = user_slot.reshape(-1)
    item_slots = item_slot.reshape(-1)
    user_fetch = gather_rows(user_table, user_picks).reshape(shard_count, cap_u, emb_width)
    item_fetch = gather_rows(item_table, item_picks).reshape(shard_count, cap_i, emb_width)
    fetched = lax.all_to_all(
        jnp.concatenate([user_fetch, item_fetch], axis=1),
        "table",
        split_axis=0,
        concat_axis=0,
        tiled=True,
    )
    user_fetched = fetched[:, :cap_u]
    item_fetched = fetched[:, cap_u:]
    user_input = pooled_input(user_fetched, user_slots, B_DEV, emb_width)
    user_state = tower_forward(user_input, user_w1, user_w2)
    item_input = pooled_input(item_fetched, item_slots, item_rows, emb_width)
    item_state = tower_forward(item_input, item_w1, item_w2)
    query_embedding_matrix = user_state[4]
    candidate_embedding_matrix = item_state[4]
    dp_index = lax.axis_index("dp")
    own_block = jnp.concatenate([query_embedding_matrix, candidate_embedding_matrix], axis=0)
    collected = lax.all_to_all(
        jnp.broadcast_to(own_block[None], (replica_count,) + own_block.shape), "dp", 0, 0
    )
    group_users = collected[:, :B_DEV].reshape(-1, emb_width)
    collected_rows = collected[:, B_DEV:].reshape(-1, emb_width)
    pairwise_match_scores = (
        jnp.dot(group_users, collected_rows.T, preferred_element_type=jnp.float32)
        / score_divisor_scale
    )
    exponent = jnp.exp(pairwise_match_scores)
    learnable_model_state = exponent / jnp.sum(exponent, axis=1, keepdims=True)
    columns = jnp.arange(replica_count * item_rows, dtype=jnp.int32)
    user_index = jnp.arange(replica_count * B_DEV, dtype=jnp.int32)
    positive = user_index // B_DEV * item_rows + user_index % B_DEV
    correct_class_indices = (columns[None, :] == positive[:, None]).astype(jnp.float32)
    score_derivative_matrix = (
        (learnable_model_state - correct_class_indices) / score_divisor_scale
    ).astype(jnp.bfloat16)
    own_rows = lax.dynamic_slice_in_dim(score_derivative_matrix, dp_index * B_DEV, B_DEV, axis=0)
    own_columns = lax.dynamic_slice_in_dim(
        score_derivative_matrix, dp_index * item_rows, item_rows, axis=1
    )
    user_emb_grad = jnp.dot(own_rows, collected_rows, preferred_element_type=jnp.float32)
    item_emb_grad = lax.dot_general(
        own_columns,
        group_users,
        (((0,), (0,)), ((), ())),
        preferred_element_type=jnp.float32,
    )
    user_back = tower_backward(
        user_input,
        user_w1,
        user_w2,
        user_state[0],
        user_state[1],
        user_state[2],
        user_state[3],
        user_emb_grad,
    )
    item_back = tower_backward(
        item_input,
        item_w1,
        item_w2,
        item_state[0],
        item_state[1],
        item_state[2],
        item_state[3],
        item_emb_grad,
    )
    weight_grads = [
        g.astype(jnp.bfloat16)
        for g in lax.psum((user_back[0], user_back[1], item_back[0], item_back[1]), ("table", "dp"))
    ]
    user_grads = gather_rows(user_back[2].reshape(-1, emb_width), user_slots).reshape(
        shard_count, cap_u, emb_width
    )
    item_grads = gather_rows(item_back[2].reshape(-1, emb_width), item_slots).reshape(
        shard_count, cap_i, emb_width
    )
    arrived = lax.all_to_all(
        jnp.concatenate([user_grads, item_grads], axis=1),
        "table",
        split_axis=0,
        concat_axis=0,
        tiled=True,
    )
    user_total = scatter_rows(user_picks, arrived[:, :cap_u].reshape(-1, emb_width), row_total)
    item_total = scatter_rows(item_picks, arrived[:, cap_u:].reshape(-1, emb_width), row_total)
    both_totals = jnp.stack(
        [
            user_total.reshape(replica_count, -1, emb_width),
            item_total.reshape(replica_count, -1, emb_width),
        ],
        axis=1,
    ).reshape(-1, emb_width)
    both_parts = lax.all_to_all(
        both_totals.reshape(replica_count, -1, emb_width), "dp", 0, 0, tiled=True
    )
    both_grads = jnp.sum(both_parts, axis=0)
    user_table_grad, item_table_grad = jnp.split(both_grads, 2, axis=0)
    return (
        user_table_grad,
        item_table_grad,
        weight_grads[0],
        weight_grads[1],
        weight_grads[2],
        weight_grads[3],
    )


def solution(mesh):
    in_specs = (
        P("table", None),
        P("table", None),
        P("table", "dp", None, None),
        P("table", "dp", None, None),
        P("table", "dp", None, None),
        P("table", "dp", None, None),
        P(),
        P(),
        P(),
        P(),
    )
    out_specs = (P(("table", "dp"), None), P(("table", "dp"), None), P(), P(), P(), P())
    return jax.shard_map(
        per_device, mesh=mesh, in_specs=in_specs, out_specs=out_specs, check_vma=False
    )
```

```python
import jax
import jax.numpy as jnp
from jax import lax
from jax.sharding import PartitionSpec as P

FEATS = 2
B_DEV = 128
NEG_DEV = 32


score_divisor_scale = 0.05
epsilon = 1e-06


def tower_forward(inputs, first_weight, second_weight):
    preact = jnp.dot(inputs, first_weight, preferred_element_type=jnp.float32)
    hidden = jnp.maximum(preact, 0.0).astype(jnp.bfloat16)
    output = jnp.dot(hidden, second_weight, preferred_element_type=jnp.float32)
    magnitude = jnp.sqrt(jnp.sum(output * output, axis=-1, keepdims=True) + epsilon)
    unit_vec = output / magnitude
    return (preact, hidden, magnitude, unit_vec, unit_vec.astype(jnp.bfloat16))


def tower_backward(
    inputs, first_weight, second_weight, preact, hidden, magnitude, unit_vec, emb_gradient
):
    along = jnp.sum(unit_vec * emb_gradient, axis=-1, keepdims=True)
    out_gradient = ((emb_gradient - unit_vec * along) / magnitude).astype(jnp.bfloat16)
    second_grad = jnp.dot(hidden.T, out_gradient, preferred_element_type=jnp.float32)
    back_hidden = jnp.dot(out_gradient, second_weight.T, preferred_element_type=jnp.float32)
    hidden_grad = jnp.where(preact > 0, back_hidden, 0.0).astype(jnp.bfloat16)
    first_grad = jnp.dot(inputs.T, hidden_grad, preferred_element_type=jnp.float32)
    input_grad = jnp.dot(hidden_grad, first_weight.T, preferred_element_type=jnp.float32).astype(
        jnp.bfloat16
    )
    return (first_grad, second_grad, input_grad)


def onehot(index, count):
    return (index[:, None] == jnp.arange(count, dtype=jnp.int32)[None, :]).astype(jnp.bfloat16)


def gather_rows(table, index):
    picked = jnp.dot(onehot(index, table.shape[0]), table, preferred_element_type=jnp.float32)
    return picked.astype(jnp.bfloat16)


def scatter_rows(index, values, count):
    return lax.dot_general(
        onehot(index, count),
        values,
        (((0,), (0,)), ((), ())),
        preferred_element_type=jnp.float32,
    )


def merged_rows(first_table, first_index, second_table, second_index):
    picked = jnp.dot(
        onehot(first_index, first_table.shape[0]), first_table, preferred_element_type=jnp.float32
    ) + jnp.dot(
        onehot(second_index, second_table.shape[0]),
        second_table,
        preferred_element_type=jnp.float32,
    )
    return picked.astype(jnp.bfloat16)


def pooled_input(fetched_rows, slot_flat, sample_count, emb_width):
    summed = scatter_rows(slot_flat, fetched_rows.reshape(-1, emb_width), sample_count * FEATS)
    return summed.astype(jnp.bfloat16).reshape(sample_count, FEATS * emb_width)


def per_device(
    user_table,
    item_table,
    user_pick,
    item_pick,
    user_slot,
    item_slot,
    user_w1,
    user_w2,
    item_w1,
    item_w2,
):
    shard_count = lax.axis_size("table")
    replica_count = lax.axis_size("dp")
    emb_width = user_table.shape[1]
    row_total = user_table.shape[0]
    item_rows = B_DEV + NEG_DEV
    cap_u = user_pick.shape[-1]
    cap_i = item_pick.shape[-1]
    def merged(user_index, item_index):
        user_part = user_index.reshape(shard_count, cap_u)
        item_part = item_index.reshape(shard_count, cap_i)
        return (
            jnp.concatenate([user_part, jnp.full_like(item_part, -1)], axis=1).reshape(-1),
            jnp.concatenate([jnp.full_like(user_part, -1), item_part], axis=1).reshape(-1),
        )

    user_picks, item_picks = merged(user_pick, item_pick)
    user_slots, item_slots = merged(user_slot, item_slot)
    fetched = lax.all_to_all(
        merged_rows(user_table, user_picks, item_table, item_picks).reshape(
            shard_count, cap_u + cap_i, emb_width
        ),
        "table",
        split_axis=0,
        concat_axis=0,
        tiled=True,
    )
    user_fetched = fetched
    item_fetched = fetched
    user_input = pooled_input(user_fetched, user_slots, B_DEV, emb_width)
    user_state = tower_forward(user_input, user_w1, user_w2)
    item_input = pooled_input(item_fetched, item_slots, item_rows, emb_width)
    item_state = tower_forward(item_input, item_w1, item_w2)
    query_embedding_matrix = user_state[4]
    candidate_embedding_matrix = item_state[4]
    dp_index = lax.axis_index("dp")
    own_block = jnp.concatenate([query_embedding_matrix, candidate_embedding_matrix], axis=0)
    collected = lax.all_to_all(
        jnp.broadcast_to(own_block[None], (replica_count,) + own_block.shape), "dp", 0, 0
    )
    group_users = collected[:, :B_DEV].reshape(-1, emb_width)
    collected_rows = collected[:, B_DEV:].reshape(-1, emb_width)
    pairwise_match_scores = (
        jnp.dot(group_users, collected_rows.T, preferred_element_type=jnp.float32)
        / score_divisor_scale
    )
    exponent = jnp.exp(pairwise_match_scores)
    learnable_model_state = exponent / jnp.sum(exponent, axis=1, keepdims=True)
    columns = jnp.arange(replica_count * item_rows, dtype=jnp.int32)
    user_index = jnp.arange(replica_count * B_DEV, dtype=jnp.int32)
    positive = user_index // B_DEV * item_rows + user_index % B_DEV
    correct_class_indices = (columns[None, :] == positive[:, None]).astype(jnp.float32)
    score_derivative_matrix = (
        (learnable_model_state - correct_class_indices) / score_divisor_scale
    ).astype(jnp.bfloat16)
    own_rows = lax.dynamic_slice_in_dim(score_derivative_matrix, dp_index * B_DEV, B_DEV, axis=0)
    own_columns = lax.dynamic_slice_in_dim(
        score_derivative_matrix, dp_index * item_rows, item_rows, axis=1
    )
    user_emb_grad = jnp.dot(own_rows, collected_rows, preferred_element_type=jnp.float32)
    item_emb_grad = lax.dot_general(
        own_columns,
        group_users,
        (((0,), (0,)), ((), ())),
        preferred_element_type=jnp.float32,
    )
    user_back = tower_backward(
        user_input,
        user_w1,
        user_w2,
        user_state[0],
        user_state[1],
        user_state[2],
        user_state[3],
        user_emb_grad,
    )
    item_back = tower_backward(
        item_input,
        item_w1,
        item_w2,
        item_state[0],
        item_state[1],
        item_state[2],
        item_state[3],
        item_emb_grad,
    )
    weight_grads = [
        g.astype(jnp.bfloat16)
        for g in lax.psum((user_back[0], user_back[1], item_back[0], item_back[1]), ("table", "dp"))
    ]
    arrived = lax.all_to_all(
        merged_rows(
            user_back[2].reshape(-1, emb_width),
            user_slots,
            item_back[2].reshape(-1, emb_width),
            item_slots,
        ).reshape(shard_count, cap_u + cap_i, emb_width),
        "table",
        split_axis=0,
        concat_axis=0,
        tiled=True,
    ).reshape(-1, emb_width)
    user_total = scatter_rows(user_picks, arrived, row_total)
    item_total = scatter_rows(item_picks, arrived, row_total)
    both_totals = jnp.stack(
        [
            user_total.reshape(replica_count, -1, emb_width),
            item_total.reshape(replica_count, -1, emb_width),
        ],
        axis=1,
    ).reshape(-1, emb_width)
    both_parts = lax.all_to_all(
        both_totals.reshape(replica_count, -1, emb_width), "dp", 0, 0, tiled=True
    )
    both_grads = jnp.sum(both_parts, axis=0)
    user_table_grad, item_table_grad = jnp.split(both_grads, 2, axis=0)
    return (
        user_table_grad,
        item_table_grad,
        weight_grads[0],
        weight_grads[1],
        weight_grads[2],
        weight_grads[3],
    )


def solution(mesh):
    in_specs = (
        P("table", None),
        P("table", None),
        P("table", "dp", None, None),
        P("table", "dp", None, None),
        P("table", "dp", None, None),
        P("table", "dp", None, None),
        P(),
        P(),
        P(),
        P(),
    )
    out_specs = (P(("table", "dp"), None), P(("table", "dp"), None), P(), P(), P(), P())
    return jax.shard_map(
        per_device, mesh=mesh, in_specs=in_specs, out_specs=out_specs, check_vma=False
    )
```

```python
import jax
import jax.numpy as jnp
from jax import lax
from jax.sharding import PartitionSpec as P

FEATS = 2
B_DEV = 128
NEG_DEV = 32


score_divisor_scale = 0.05
epsilon = 1e-06


def tower_forward(inputs, first_weight, second_weight):
    preact = jnp.dot(inputs, first_weight, preferred_element_type=jnp.float32)
    hidden = jnp.maximum(preact, 0.0).astype(jnp.bfloat16)
    output = jnp.dot(hidden, second_weight, preferred_element_type=jnp.float32)
    magnitude = jnp.sqrt(jnp.sum(output * output, axis=-1, keepdims=True) + epsilon)
    unit_vec = output / magnitude
    return (preact, hidden, magnitude, unit_vec, unit_vec.astype(jnp.bfloat16))


def tower_backward(
    inputs, first_weight, second_weight, preact, hidden, magnitude, unit_vec, emb_gradient
):
    along = jnp.sum(unit_vec * emb_gradient, axis=-1, keepdims=True)
    out_gradient = ((emb_gradient - unit_vec * along) / magnitude).astype(jnp.bfloat16)
    second_grad = jnp.dot(hidden.T, out_gradient, preferred_element_type=jnp.float32)
    back_hidden = jnp.dot(out_gradient, second_weight.T, preferred_element_type=jnp.float32)
    hidden_grad = jnp.where(preact > 0, back_hidden, 0.0).astype(jnp.bfloat16)
    first_grad = jnp.dot(inputs.T, hidden_grad, preferred_element_type=jnp.float32)
    input_grad = jnp.dot(hidden_grad, first_weight.T, preferred_element_type=jnp.float32).astype(
        jnp.bfloat16
    )
    return (first_grad, second_grad, input_grad)


def onehot(index, count):
    return (index[:, None] == jnp.arange(count, dtype=jnp.int32)[None, :]).astype(jnp.bfloat16)


def gather_rows(table, index):
    picked = jnp.dot(onehot(index, table.shape[0]), table, preferred_element_type=jnp.float32)
    return picked.astype(jnp.bfloat16)


def scatter_rows(index, values, count):
    return lax.dot_general(
        onehot(index, count),
        values,
        (((0,), (0,)), ((), ())),
        preferred_element_type=jnp.float32,
    )


def pooled_input(fetched_rows, slot_flat, sample_count, emb_width):
    summed = scatter_rows(slot_flat, fetched_rows.reshape(-1, emb_width), sample_count * FEATS)
    return summed.astype(jnp.bfloat16).reshape(sample_count, FEATS * emb_width)


def per_device(
    user_table,
    item_table,
    user_pick,
    item_pick,
    user_slot,
    item_slot,
    user_w1,
    user_w2,
    item_w1,
    item_w2,
):
    shard_count = lax.axis_size("table")
    replica_count = lax.axis_size("dp")
    emb_width = user_table.shape[1]
    row_total = user_table.shape[0]
    item_rows = B_DEV + NEG_DEV
    cap_u = user_pick.shape[-1]
    cap_i = item_pick.shape[-1]
    user_picks = user_pick.reshape(-1)
    item_picks = item_pick.reshape(-1)
    user_slots = user_slot.reshape(-1)
    item_slots = item_slot.reshape(-1)
    user_fetch = gather_rows(user_table, user_picks).reshape(shard_count, cap_u, emb_width)
    item_fetch = gather_rows(item_table, item_picks).reshape(shard_count, cap_i, emb_width)
    fetched = lax.all_to_all(
        jnp.concatenate([user_fetch, item_fetch], axis=1),
        "table",
        split_axis=0,
        concat_axis=0,
        tiled=True,
    )
    user_fetched = fetched[:, :cap_u]
    item_fetched = fetched[:, cap_u:]
    user_input = pooled_input(user_fetched, user_slots, B_DEV, emb_width)
    user_state = tower_forward(user_input, user_w1, user_w2)
    item_input = pooled_input(item_fetched, item_slots, item_rows, emb_width)
    item_state = tower_forward(item_input, item_w1, item_w2)
    query_embedding_matrix = user_state[4]
    candidate_embedding_matrix = item_state[4]
    dp_index = lax.axis_index("dp")
    own_block = jnp.concatenate([query_embedding_matrix, candidate_embedding_matrix], axis=0)
    collected = lax.all_to_all(
        jnp.broadcast_to(own_block[None], (replica_count,) + own_block.shape), "dp", 0, 0
    )
    group_users = collected[:, :B_DEV].reshape(-1, emb_width)
    collected_rows = collected[:, B_DEV:].reshape(-1, emb_width)
    pairwise_match_scores = (
        jnp.dot(group_users, collected_rows.T, preferred_element_type=jnp.float32)
        / score_divisor_scale
    )
    exponent = jnp.exp(pairwise_match_scores)
    learnable_model_state = exponent / jnp.sum(exponent, axis=1, keepdims=True)
    columns = jnp.arange(replica_count * item_rows, dtype=jnp.int32)
    user_index = jnp.arange(replica_count * B_DEV, dtype=jnp.int32)
    positive = user_index // B_DEV * item_rows + user_index % B_DEV
    correct_class_indices = (columns[None, :] == positive[:, None]).astype(jnp.float32)
    score_derivative_matrix = (
        (learnable_model_state - correct_class_indices) / score_divisor_scale
    ).astype(jnp.bfloat16)
    own_rows = lax.dynamic_slice_in_dim(score_derivative_matrix, dp_index * B_DEV, B_DEV, axis=0)
    own_columns = lax.dynamic_slice_in_dim(
        score_derivative_matrix, dp_index * item_rows, item_rows, axis=1
    )
    user_emb_grad = jnp.dot(own_rows, collected_rows, preferred_element_type=jnp.float32)
    item_emb_grad = lax.dot_general(
        own_columns,
        group_users,
        (((0,), (0,)), ((), ())),
        preferred_element_type=jnp.float32,
    )
    user_back = tower_backward(
        user_input,
        user_w1,
        user_w2,
        user_state[0],
        user_state[1],
        user_state[2],
        user_state[3],
        user_emb_grad,
    )
    item_back = tower_backward(
        item_input,
        item_w1,
        item_w2,
        item_state[0],
        item_state[1],
        item_state[2],
        item_state[3],
        item_emb_grad,
    )
    weight_grads = [
        g.astype(jnp.bfloat16)
        for g in lax.psum((user_back[0], user_back[1], item_back[0], item_back[1]), ("table", "dp"))
    ]
    user_grads = gather_rows(user_back[2].reshape(-1, emb_width), user_slots).reshape(
        shard_count, cap_u, emb_width
    )
    item_grads = gather_rows(item_back[2].reshape(-1, emb_width), item_slots).reshape(
        shard_count, cap_i, emb_width
    )
    arrived = lax.all_to_all(
        jnp.concatenate([user_grads, item_grads], axis=1),
        "table",
        split_axis=0,
        concat_axis=0,
        tiled=True,
    )
    arrived, weight_grads = lax.optimization_barrier((arrived, weight_grads))
    user_total = scatter_rows(user_picks, arrived[:, :cap_u].reshape(-1, emb_width), row_total)
    item_total = scatter_rows(item_picks, arrived[:, cap_u:].reshape(-1, emb_width), row_total)
    both_totals = jnp.stack(
        [
            user_total.reshape(replica_count, -1, emb_width),
            item_total.reshape(replica_count, -1, emb_width),
        ],
        axis=1,
    ).reshape(-1, emb_width)
    both_parts = lax.all_to_all(
        both_totals.reshape(replica_count, -1, emb_width), "dp", 0, 0, tiled=True
    )
    both_grads = jnp.sum(both_parts, axis=0)
    user_table_grad, item_table_grad = jnp.split(both_grads, 2, axis=0)
    return (
        user_table_grad,
        item_table_grad,
        weight_grads[0],
        weight_grads[1],
        weight_grads[2],
        weight_grads[3],
    )


def solution(mesh):
    in_specs = (
        P("table", None),
        P("table", None),
        P("table", "dp", None, None),
        P("table", "dp", None, None),
        P("table", "dp", None, None),
        P("table", "dp", None, None),
        P(),
        P(),
        P(),
        P(),
    )
    out_specs = (P(("table", "dp"), None), P(("table", "dp"), None), P(), P(), P(), P())
    return jax.shard_map(
        per_device, mesh=mesh, in_specs=in_specs, out_specs=out_specs, check_vma=False
    )
```

```python
import jax
import jax.numpy as jnp
from jax import lax
from jax.sharding import PartitionSpec as P

FEATS = 2
B_DEV = 128
NEG_DEV = 32


score_divisor_scale = 0.05
epsilon = 1e-06


def tower_forward(inputs, first_weight, second_weight):
    preact = jnp.dot(inputs, first_weight, preferred_element_type=jnp.float32)
    hidden = jnp.maximum(preact, 0.0).astype(jnp.bfloat16)
    output = jnp.dot(hidden, second_weight, preferred_element_type=jnp.float32)
    magnitude = jnp.sqrt(jnp.sum(output * output, axis=-1, keepdims=True) + epsilon)
    unit_vec = output / magnitude
    return (preact, hidden, magnitude, unit_vec, unit_vec.astype(jnp.bfloat16))


def tower_backward(
    inputs, first_weight, second_weight, preact, hidden, magnitude, unit_vec, emb_gradient
):
    along = jnp.sum(unit_vec * emb_gradient, axis=-1, keepdims=True)
    out_gradient = ((emb_gradient - unit_vec * along) / magnitude).astype(jnp.bfloat16)
    second_grad = jnp.dot(hidden.T, out_gradient, preferred_element_type=jnp.float32)
    back_hidden = jnp.dot(out_gradient, second_weight.T, preferred_element_type=jnp.float32)
    hidden_grad = jnp.where(preact > 0, back_hidden, 0.0).astype(jnp.bfloat16)
    first_grad = jnp.dot(inputs.T, hidden_grad, preferred_element_type=jnp.float32)
    input_grad = jnp.dot(hidden_grad, first_weight.T, preferred_element_type=jnp.float32).astype(
        jnp.bfloat16
    )
    return (first_grad, second_grad, input_grad)


def onehot(index, count):
    return (index[:, None] == jnp.arange(count, dtype=jnp.int32)[None, :]).astype(jnp.bfloat16)


def gather_rows(table, index):
    picked = jnp.dot(onehot(index, table.shape[0]), table, preferred_element_type=jnp.float32)
    return picked.astype(jnp.bfloat16)


def scatter_rows(index, values, count):
    return lax.dot_general(
        onehot(index, count),
        values,
        (((0,), (0,)), ((), ())),
        preferred_element_type=jnp.float32,
    )


def merged_rows(first_table, first_index, second_table, second_index):
    picked = jnp.dot(
        onehot(first_index, first_table.shape[0]), first_table, preferred_element_type=jnp.float32
    ) + jnp.dot(
        onehot(second_index, second_table.shape[0]),
        second_table,
        preferred_element_type=jnp.float32,
    )
    return picked.astype(jnp.bfloat16)


def pooled_input(fetched_rows, slot_flat, sample_count, emb_width):
    summed = scatter_rows(slot_flat, fetched_rows.reshape(-1, emb_width), sample_count * FEATS)
    return summed.astype(jnp.bfloat16).reshape(sample_count, FEATS * emb_width)


def per_device(
    user_table,
    item_table,
    user_pick,
    item_pick,
    user_slot,
    item_slot,
    user_w1,
    user_w2,
    item_w1,
    item_w2,
):
    shard_count = lax.axis_size("table")
    replica_count = lax.axis_size("dp")
    emb_width = user_table.shape[1]
    row_total = user_table.shape[0]
    item_rows = B_DEV + NEG_DEV
    cap_u = user_pick.shape[-1]
    cap_i = item_pick.shape[-1]
    def merged(user_index, item_index):
        user_part = user_index.reshape(shard_count, cap_u)
        item_part = item_index.reshape(shard_count, cap_i)
        return (
            jnp.concatenate([user_part, jnp.full_like(item_part, -1)], axis=1).reshape(-1),
            jnp.concatenate([jnp.full_like(user_part, -1), item_part], axis=1).reshape(-1),
        )

    user_picks, item_picks = merged(user_pick, item_pick)
    user_slots, item_slots = merged(user_slot, item_slot)
    fetched = lax.all_to_all(
        merged_rows(user_table, user_picks, item_table, item_picks).reshape(
            shard_count, cap_u + cap_i, emb_width
        ),
        "table",
        split_axis=0,
        concat_axis=0,
        tiled=True,
    )
    user_fetched = fetched
    item_fetched = fetched
    user_input = pooled_input(user_fetched, user_slots, B_DEV, emb_width)
    user_state = tower_forward(user_input, user_w1, user_w2)
    item_input = pooled_input(item_fetched, item_slots, item_rows, emb_width)
    item_state = tower_forward(item_input, item_w1, item_w2)
    query_embedding_matrix = user_state[4]
    candidate_embedding_matrix = item_state[4]
    dp_index = lax.axis_index("dp")
    own_block = jnp.concatenate([query_embedding_matrix, candidate_embedding_matrix], axis=0)
    collected = lax.all_to_all(
        jnp.broadcast_to(own_block[None], (replica_count,) + own_block.shape), "dp", 0, 0
    )
    group_users = collected[:, :B_DEV].reshape(-1, emb_width)
    collected_rows = collected[:, B_DEV:].reshape(-1, emb_width)
    pairwise_match_scores = (
        jnp.dot(group_users, collected_rows.T, preferred_element_type=jnp.float32)
        / score_divisor_scale
    )
    exponent = jnp.exp(pairwise_match_scores)
    learnable_model_state = exponent / jnp.sum(exponent, axis=1, keepdims=True)
    columns = jnp.arange(replica_count * item_rows, dtype=jnp.int32)
    user_index = jnp.arange(replica_count * B_DEV, dtype=jnp.int32)
    positive = user_index // B_DEV * item_rows + user_index % B_DEV
    correct_class_indices = (columns[None, :] == positive[:, None]).astype(jnp.float32)
    score_derivative_matrix = (
        (learnable_model_state - correct_class_indices) / score_divisor_scale
    ).astype(jnp.bfloat16)
    own_rows = lax.dynamic_slice_in_dim(score_derivative_matrix, dp_index * B_DEV, B_DEV, axis=0)
    own_columns = lax.dynamic_slice_in_dim(
        score_derivative_matrix, dp_index * item_rows, item_rows, axis=1
    )
    user_emb_grad = jnp.dot(own_rows, collected_rows, preferred_element_type=jnp.float32)
    item_emb_grad = lax.dot_general(
        own_columns,
        group_users,
        (((0,), (0,)), ((), ())),
        preferred_element_type=jnp.float32,
    )
    user_back = tower_backward(
        user_input,
        user_w1,
        user_w2,
        user_state[0],
        user_state[1],
        user_state[2],
        user_state[3],
        user_emb_grad,
    )
    item_back = tower_backward(
        item_input,
        item_w1,
        item_w2,
        item_state[0],
        item_state[1],
        item_state[2],
        item_state[3],
        item_emb_grad,
    )
    weight_grads = [
        g.astype(jnp.bfloat16)
        for g in lax.psum((user_back[0], user_back[1], item_back[0], item_back[1]), ("table", "dp"))
    ]
    arrived = lax.all_to_all(
        merged_rows(
            user_back[2].reshape(-1, emb_width),
            user_slots,
            item_back[2].reshape(-1, emb_width),
            item_slots,
        ).reshape(shard_count, cap_u + cap_i, emb_width),
        "table",
        split_axis=0,
        concat_axis=0,
        tiled=True,
    ).reshape(-1, emb_width)
    arrived, weight_grads = lax.optimization_barrier((arrived, weight_grads))
    user_total = scatter_rows(user_picks, arrived, row_total)
    item_total = scatter_rows(item_picks, arrived, row_total)
    both_totals = jnp.stack(
        [
            user_total.reshape(replica_count, -1, emb_width),
            item_total.reshape(replica_count, -1, emb_width),
        ],
        axis=1,
    ).reshape(-1, emb_width)
    both_parts = lax.all_to_all(
        both_totals.reshape(replica_count, -1, emb_width), "dp", 0, 0, tiled=True
    )
    both_grads = jnp.sum(both_parts, axis=0)
    user_table_grad, item_table_grad = jnp.split(both_grads, 2, axis=0)
    return (
        user_table_grad,
        item_table_grad,
        weight_grads[0],
        weight_grads[1],
        weight_grads[2],
        weight_grads[3],
    )


def solution(mesh):
    in_specs = (
        P("table", None),
        P("table", None),
        P("table", "dp", None, None),
        P("table", "dp", None, None),
        P("table", "dp", None, None),
        P("table", "dp", None, None),
        P(),
        P(),
        P(),
        P(),
    )
    out_specs = (P(("table", "dp"), None), P(("table", "dp"), None), P(), P(), P(), P())
    return jax.shard_map(
        per_device, mesh=mesh, in_specs=in_specs, out_specs=out_specs, check_vma=False
    )
```
